512 devices in a mesh: rows: 32 (over y, x), vocab: 16 (over z, core).
Axes of the slice: x: 4, y: 8, z: 8, core: 2. Of those that a mesh axis runs over, the one named last changes fastest.
Arguments:
- hidden: bfloat16 [12288, 8192], P('rows', 'vocab'), may hold values from -128 to 128
- head: bfloat16 [8192, 8192], P('rows', 'vocab'), may hold values from -4 to 4
- targets: int32 [12288], P('rows'), may hold values from 0 to 128255
- live: int32 [12288], P('rows'), may hold values from 0 to 1, as said below
- prior_lse: float32 [12288], P('rows'), may hold values from 10 to 18
- prior_mean: float32 [12288], P('rows'), may hold values from 2 to 8
- prior_target: float32 [12288], P('rows'), may hold values from -12 to 12
- seq_lengths: int32 [32], replicated, may hold values from 1 to 768, 12288 in all
Outputs:
- logprob: float32 [12288], P(('rows', 'vocab'))
- entropy: float32 [12288], P(('rows', 'vocab'))
- seq_score: float32 [32], replicated
The draws below stay inside these ranges and needn't reach their ends.
Inputs may be any that keep to these rules, and one draw needn't show every extreme that they name: Within the 384 rows of each index of rows, the live rows come first; every such index has at least 48 live rows and some index has all 384.
All inputs are finite; a program needn't handle non-finite values.
Results may differ from the reference program's by a relative error of at most 0.0003.
Values may be sent and summed in bfloat16 or wider, within the bound.
No kernel may reach another device: no remote copies, remote signals or barrier semaphores. Data moves between devices by JAX's collectives and lax.ppermute only.
A program may use at most 64 MiB of HBM per device.

```python
import math
import jax
import jax.numpy as jnp
import numpy as np
from jax import lax

D = 8192
VOCAB = 128256
ROW_DEV = 384
SEQS = 32
GSIZE = 8
ROWS = 12288
VB_ALL = 8192
VSTART = 120064


def head_values(key):
    base = jax.random.fold_in(key, 11)
    first_key, second_key = jax.random.split(base)
    scales = jnp.exp(jax.random.uniform(second_key, (VB_ALL,), jnp.float32, math.log(0.5), math.log(2.0)))
    values = jnp.clip(jax.random.normal(first_key, (D, VB_ALL), jnp.float32), -6.0, 6.0)
    return values * (2.0 / math.sqrt(D)) * scales[None, :]


def draw_head(key, part):
    return head_values(key).astype(jnp.bfloat16)


def draw_hidden(key, part):
    base = jax.random.fold_in(key, 23)
    value_key, scale_key = jax.random.split(base, 2)
    row_scale = jnp.exp(jax.random.uniform(scale_key, (ROWS, 1), jnp.float32, math.log(0.5), math.log(2.0)))
    values = jnp.clip(jax.random.normal(value_key, (ROWS, D), jnp.float32), -6.0, 6.0) * row_scale
    return values.astype(jnp.bfloat16)


def draw_live(key, part):
    count_key, full_key = jax.random.split(jax.random.fold_in(key, 37))
    devices = ROWS // ROW_DEV
    counts = jax.random.randint(count_key, (devices,), ROW_DEV // 8, ROW_DEV // 2 + 1)
    fullest = jax.random.randint(full_key, (), 0, devices)
    counts = jnp.where(jnp.arange(devices) == fullest, ROW_DEV, counts)
    position = jnp.arange(ROWS, dtype=jnp.int32) % ROW_DEV
    owner = jnp.arange(ROWS, dtype=jnp.int32) // ROW_DEV
    return (position < counts[owner]).astype(jnp.int32)


def draw_targets(key, part):
    side_key, inner_key, outer_key = jax.random.split(jax.random.fold_in(key, 53), 3)
    inside = jax.random.randint(side_key, (ROWS,), 0, 2)
    in_block = jax.random.randint(inner_key, (ROWS,), VSTART, VOCAB)
    earlier = jax.random.randint(outer_key, (ROWS,), 0, VSTART)
    chosen = jnp.where(inside == 1, in_block, earlier)
    return chosen.at[0].set(0).at[1].set(VOCAB - 1).astype(jnp.int32)


def block_scale(rng, dims, cuts, least, top_value):
    def one(axis_at, parts):
        heights = jax.random.uniform(jax.random.fold_in(jax.random.fold_in(rng, 6), axis_at), (parts,), jnp.float32, least / len(cuts), top_value / len(cuts))
        return jnp.repeat(jnp.exp(heights), dims[axis_at] // parts).reshape((-1,) + (1,) * (len(dims) - axis_at - 1))

    loudness = one(*cuts[0])
    for cut in cuts[1:]:
        loudness = loudness * one(*cut)
    return loudness


def length_profile(number_of, total, bound, lean):
    weights = [(1 << 20) // math.isqrt(standing ** lean) + 1 for standing in range(2, number_of + 1)]
    surplus, holding = total - bound - (number_of - 1), [1] * (number_of - 1)
    while surplus > 0:
        free = [i for i in range(number_of - 1) if holding[i] < bound]
        mass, remaining = sum([weights[i] for i in free]), surplus
        for i in free:
            extra = min(bound - holding[i], max(1, remaining * weights[i] // mass), surplus)
            holding[i] = holding[i] + extra
            surplus = surplus - extra
    return np.array([bound] + holding)


def uneven(rng, number_of, total, most, skew):
    if number_of == 2:
        one = jax.random.randint(rng, (), max(1, total - most), min(most, total - 1) + 1)
        return jnp.stack([one, total - one])
    lengths = jnp.asarray(length_profile(number_of, total, most, skew), jnp.int32)
    twos = (number_of - 1) // 2
    giver, receiver = lengths[1:1 + 2 * twos:2], lengths[2:2 + 2 * twos:2]
    slack = jnp.minimum(giver - 1, most - receiver)
    moved = jax.random.randint(jax.random.fold_in(rng, 1), (twos,), 0, 1 << 20) % (slack + 1)
    lengths = lengths.at[1:1 + 2 * twos:2].set(giver - moved).at[2:2 + 2 * twos:2].set(receiver + moved)
    return lengths[jax.random.permutation(jax.random.fold_in(rng, 2), number_of)]


def scatter_about(own_key, dims, spread, reach, shards=(), held_as=jnp.bfloat16):
    result = jax.random.normal(own_key, dims, jnp.float32) * spread
    if len(shards) > 0:
        result = block_scale(own_key, dims, shards, -0.22, 0.18) * result
    return jnp.clip(result, min=-reach, max=reach).astype(held_as)


def setup_inputs(seed: int = 0) -> dict:
    keys = jax.random.split(jax.random.key(seed), 9)
    hidden = draw_hidden(jax.random.fold_in(keys[8], 71), 0)
    head = draw_head(jax.random.fold_in(keys[8], 71), 0)
    targets = draw_targets(jax.random.fold_in(keys[8], 71), 0)
    live = draw_live(jax.random.fold_in(keys[8], 71), 0)
    prior_lse = jnp.clip(10.0 + 8.0 * jax.random.uniform(keys[4], (ROWS,), jnp.float32) ** block_scale(keys[4], (ROWS,), ((0, 32),), -0.2, 0.2), 10.0, 18.0)
    prior_mean = jnp.clip(2.0 + 6.0 * jax.random.uniform(keys[5], (ROWS,), jnp.float32) ** block_scale(keys[5], (ROWS,), ((0, 32),), -0.2, 0.2), 2.0, 8.0)
    prior_target = scatter_about(keys[6], (ROWS,), 3.0, 12.0, ((0, 32),), jnp.float32)
    seq_lengths = uneven(keys[7], SEQS, ROWS, 2 * ROWS // SEQS, 2).astype(jnp.int32)
    return {"hidden": hidden, "head": head, "targets": targets, "live": live, "prior_lse": prior_lse, "prior_mean": prior_mean, "prior_target": prior_target, "seq_lengths": seq_lengths}


def finish_rows(block_peak, block_mass, block_moment, block_target, live, prior_lse, prior_mean):
    highest = jnp.maximum(block_peak, prior_lse)
    earlier = jnp.exp(prior_lse - highest)
    scaled = jnp.exp(block_peak - highest)
    total_mass = earlier + block_mass * scaled
    norm_log = highest + jnp.log(total_mass)
    average = (earlier * prior_mean + scaled * block_moment) / total_mass
    keeping = live.astype(jnp.float32)
    return keeping * (block_target - norm_log), keeping * (norm_log - average)


def reference(hidden, head, targets, live, prior_lse, prior_mean, prior_target, seq_lengths):
    blocks = ROWS // ROW_DEV

    def block_stats(operands):
        row_block, chosen = operands
        logits = jnp.dot(row_block, head, preferred_element_type=jnp.float32)
        row_peak = jnp.max(logits, axis=1)
        weights = jnp.exp(logits - row_peak[:, None])
        row_mass = jnp.sum(weights, axis=1)
        moment = jnp.sum(weights * logits, axis=1)
        column = chosen - VSTART
        columns = jnp.arange(VB_ALL, dtype=jnp.int32)
        picked = jnp.sum(jnp.where(columns[None, :] == column[:, None], logits, jnp.zeros_like(logits)), axis=1)
        return row_peak, row_mass, moment, picked

    row_peak, row_mass, moment, picked = lax.map(block_stats, (hidden.reshape(blocks, ROW_DEV, D), targets.reshape(blocks, ROW_DEV)))
    row_peak = row_peak.reshape(ROWS)
    row_mass = row_mass.reshape(ROWS)
    moment = moment.reshape(ROWS)
    picked = picked.reshape(ROWS)
    block_target = jnp.where(targets >= VSTART, picked, prior_target)
    logprob, entropy = finish_rows(row_peak, row_mass, moment, block_target, live, prior_lse, prior_mean)
    endings = jnp.cumsum(seq_lengths)
    positions = jnp.arange(ROWS, dtype=jnp.int32)
    member = jnp.sum((positions[:, None] >= endings[None, :]).astype(jnp.int32), axis=1)
    onehot = (member[:, None] == jnp.arange(SEQS, dtype=jnp.int32)[None, :]).astype(jnp.float32)
    sums = jnp.sum(onehot * logprob[:, None], axis=0)
    seq_mean = sums / seq_lengths.astype(jnp.float32)
    grouped = seq_mean.reshape(SEQS // GSIZE, GSIZE)
    seq_score = (grouped - jnp.mean(grouped, axis=1, keepdims=True)).reshape(SEQS)
    return logprob, entropy, seq_score
```

```python
import jax
import jax.numpy as jnp
from jax import lax
from jax.sharding import PartitionSpec as P

VOCAB = 128256
SEQS = 32
GSIZE = 8


def finish_rows(block_peak, block_mass, block_moment, block_target, live, prior_lse, prior_mean):
    highest = jnp.maximum(block_peak, prior_lse)
    earlier = jnp.exp(prior_lse - highest)
    scaled = jnp.exp(block_peak - highest)
    total_mass = earlier + block_mass * scaled
    norm_log = highest + jnp.log(total_mass)
    average = (earlier * prior_mean + scaled * block_moment) / total_mass
    keeping = live.astype(jnp.float32)
    return (keeping * (block_target - norm_log), keeping * (norm_log - average))


def local(hidden, head, targets, live, prior_lse, prior_mean, prior_target, seq_lengths):
    rows_here = hidden.shape[0]
    cols_here = head.shape[1]
    spread = lax.axis_size("vocab")
    which = lax.axis_index("vocab")
    block_first = VOCAB - cols_here * spread
    first_col = block_first + which * cols_here
    gathered = lax.all_gather(hidden, "vocab", axis=1, tiled=True)
    logits = jnp.dot(
        gathered,
        lax.all_gather(head, "rows", axis=0, tiled=True),
        preferred_element_type=jnp.float32,
    )
    row_peak = jnp.max(logits, axis=1)
    weights = jnp.exp(logits - row_peak[:, None])
    row_mass = jnp.sum(weights, axis=1)
    moment = jnp.sum(weights * logits, axis=1)
    column = targets - first_col
    columns = lax.broadcasted_iota(jnp.int32, logits.shape, 1)
    picked = jnp.sum(jnp.where(columns == column[:, None], logits, jnp.zeros_like(logits)), axis=1)

    stats = jnp.stack([row_peak, row_mass, moment, picked])
    every = lax.all_gather(stats, "vocab", axis=0, tiled=False)
    peaks = every[:, 0]
    highest = jnp.max(peaks, axis=0)
    factor = jnp.exp(peaks - highest[None, :])
    mass_all = jnp.sum(every[:, 1] * factor, axis=0)
    moment_all = jnp.sum(every[:, 2] * factor, axis=0)
    picked_all = jnp.sum(every[:, 3], axis=0)
    block_target = jnp.where(targets >= block_first, picked_all, prior_target)
    logprob, entropy = finish_rows(
        highest, mass_all, moment_all, block_target, live, prior_lse, prior_mean
    )

    share = rows_here // spread
    begin = which * share
    logprob_share = lax.dynamic_slice_in_dim(logprob, begin, share, 0)
    entropy_share = lax.dynamic_slice_in_dim(entropy, begin, share, 0)

    global_rows = lax.axis_index("rows") * rows_here + jnp.arange(rows_here, dtype=jnp.int32)
    endings = jnp.cumsum(seq_lengths)
    member = jnp.sum((global_rows[:, None] >= endings[None, :]).astype(jnp.int32), axis=1)
    onehot = (member[:, None] == jnp.arange(SEQS, dtype=jnp.int32)[None, :]).astype(jnp.float32)
    partial_sums = jnp.sum(onehot * logprob[:, None], axis=0)
    sums = jnp.sum(lax.all_gather(partial_sums, "rows", axis=0, tiled=False), axis=0)
    seq_mean = sums / seq_lengths.astype(jnp.float32)
    grouped = seq_mean.reshape(SEQS // GSIZE, GSIZE)
    seq_score = (grouped - jnp.mean(grouped, axis=1, keepdims=True)).reshape(SEQS)
    return (logprob_share, entropy_share, seq_score)


def solution(mesh):
    return jax.shard_map(
        local,
        mesh=mesh,
        in_specs=(
            P("rows", "vocab"),
            P("rows", "vocab"),
            P("rows"),
            P("rows"),
            P("rows"),
            P("rows"),
            P("rows"),
            P(),
        ),
        out_specs=(P(("rows", "vocab")), P(("rows", "vocab")), P()),
        check_vma=False,
    )
```

```python
import jax
import jax.numpy as jnp
from jax import lax
from jax.sharding import PartitionSpec as P

VOCAB = 128256
SEQS = 32
GSIZE = 8
ROW_AXES = ("y", "x")
VOCAB_AXES = ("z", "c")


def finish_rows(block_peak, block_mass, block_moment, block_target, live, prior_lse, prior_mean):
    highest = jnp.maximum(block_peak, prior_lse)
    earlier = jnp.exp(prior_lse - highest)
    scaled = jnp.exp(block_peak - highest)
    total_mass = earlier + block_mass * scaled
    norm_log = highest + jnp.log(total_mass)
    average = (earlier * prior_mean + scaled * block_moment) / total_mass
    keeping = live.astype(jnp.float32)
    return (keeping * (block_target - norm_log), keeping * (norm_log - average))


def local(hidden, head, targets, live, prior_lse, prior_mean, prior_target, seq_lengths):
    rows_here = hidden.shape[0]
    cols_here = head.shape[1]
    spread = lax.axis_size(VOCAB_AXES)
    which = lax.axis_index(VOCAB_AXES)
    block_first = VOCAB - cols_here * spread
    first_col = block_first + which * cols_here
    gathered = lax.all_gather(hidden, VOCAB_AXES, axis=1, tiled=True)
    logits = jnp.dot(
        gathered,
        lax.all_gather(head, ROW_AXES, axis=0, tiled=True),
        preferred_element_type=jnp.float32,
    )
    row_peak = jnp.max(logits, axis=1)
    weights = jnp.exp(logits - row_peak[:, None])
    row_mass = jnp.sum(weights, axis=1)
    moment = jnp.sum(weights * logits, axis=1)
    column = targets - first_col
    columns = lax.broadcasted_iota(jnp.int32, logits.shape, 1)
    picked = jnp.sum(jnp.where(columns == column[:, None], logits, jnp.zeros_like(logits)), axis=1)

    stats = jnp.stack([row_peak, row_mass, moment, picked])
    every = lax.all_gather(stats, VOCAB_AXES, axis=0, tiled=False)
    peaks = every[:, 0]
    highest = jnp.max(peaks, axis=0)
    factor = jnp.exp(peaks - highest[None, :])
    mass_all = jnp.sum(every[:, 1] * factor, axis=0)
    moment_all = jnp.sum(every[:, 2] * factor, axis=0)
    picked_all = jnp.sum(every[:, 3], axis=0)
    block_target = jnp.where(targets >= block_first, picked_all, prior_target)
    logprob, entropy = finish_rows(
        highest, mass_all, moment_all, block_target, live, prior_lse, prior_mean
    )

    share = rows_here // spread
    begin = which * share
    logprob_share = lax.dynamic_slice_in_dim(logprob, begin, share, 0)
    entropy_share = lax.dynamic_slice_in_dim(entropy, begin, share, 0)

    global_rows = lax.axis_index(ROW_AXES) * rows_here + jnp.arange(rows_here, dtype=jnp.int32)
    endings = jnp.cumsum(seq_lengths)
    member = jnp.sum((global_rows[:, None] >= endings[None, :]).astype(jnp.int32), axis=1)
    onehot = (member[:, None] == jnp.arange(SEQS, dtype=jnp.int32)[None, :]).astype(jnp.float32)
    partial_sums = jnp.sum(onehot * logprob[:, None], axis=0)
    sums = lax.psum(lax.psum(partial_sums, "x"), "y")
    seq_mean = sums / seq_lengths.astype(jnp.float32)
    grouped = seq_mean.reshape(SEQS // GSIZE, GSIZE)
    seq_score = (grouped - jnp.mean(grouped, axis=1, keepdims=True)).reshape(SEQS)
    return (logprob_share, entropy_share, seq_score)


def solution(mesh):
    rows_y = 8 if mesh.shape["rows"] % 8 == 0 else 1
    vocab_c = 2 if mesh.shape["vocab"] % 2 == 0 else 1
    devices = mesh.devices.reshape(
        rows_y, mesh.shape["rows"] // rows_y, mesh.shape["vocab"] // vocab_c, vocab_c
    )
    fine = jax.sharding.Mesh(devices, ("y", "x", "z", "c"))
    rows, vocab = ROW_AXES, VOCAB_AXES
    return jax.shard_map(
        local,
        mesh=fine,
        in_specs=(
            P(rows, vocab),
            P(rows, vocab),
            P(rows),
            P(rows),
            P(rows),
            P(rows),
            P(rows),
            P(),
        ),
        out_specs=(P(rows + vocab), P(rows + vocab), P()),
        check_vma=False,
    )
```

```python
import jax
import jax.numpy as jnp
from jax import lax
from jax.sharding import PartitionSpec as P

VOCAB = 128256
SEQS = 32
GSIZE = 8
ROW_AXES = ("y", "x")
VOCAB_AXES = ("z", "c")


def finish_rows(block_peak, block_mass, block_moment, block_target, live, prior_lse, prior_mean):
    highest = jnp.maximum(block_peak, prior_lse)
    earlier = jnp.exp(prior_lse - highest)
    scaled = jnp.exp(block_peak - highest)
    total_mass = earlier + block_mass * scaled
    norm_log = highest + jnp.log(total_mass)
    average = (earlier * prior_mean + scaled * block_moment) / total_mass
    keeping = live.astype(jnp.float32)
    return (keeping * (block_target - norm_log), keeping * (norm_log - average))


def gather_hidden(hidden):
    nz = lax.axis_size("z")
    z = lax.axis_index("z")
    c = lax.axis_index("c")
    nc = lax.axis_size("c")
    width = hidden.shape[1]
    ahead = [(i, (i + 1) % nz) for i in range(nz)]
    behind = [(i, (i - 1) % nz) for i in range(nz)]
    across = [(i, (i + 1) % nc) for i in range(nc)]
    full = jnp.zeros((hidden.shape[0], width * nz * nc), hidden.dtype)

    def place(buf, piece, chip, core):
        slot = (chip * nc + core) * width
        return lax.dynamic_update_slice(buf, piece, (0, slot))

    def share(buf, piece, chip):
        buf = place(buf, piece, chip, c)
        if nc > 1:
            other = lax.ppermute(piece, "c", across)
            buf = place(buf, other, chip, (c + 1) % nc)
        return buf

    full = share(full, hidden, z)
    fwd = hidden
    bwd = hidden
    for step in range(1, nz // 2 + 1):
        fwd = lax.ppermute(fwd, "z", ahead)
        if step <= (nz - 1) // 2:
            bwd = lax.ppermute(bwd, "z", behind)
        full = share(full, fwd, (z - step) % nz)
        if step <= (nz - 1) // 2:
            full = share(full, bwd, (z + step) % nz)
    return full


def local(hidden, head, targets, live, prior_lse, prior_mean, prior_target, seq_lengths):
    rows_here = hidden.shape[0]
    cols_here = head.shape[1]
    spread = lax.axis_size(VOCAB_AXES)
    which = lax.axis_index(VOCAB_AXES)
    block_first = VOCAB - cols_here * spread
    first_col = block_first + which * cols_here
    gathered = gather_hidden(hidden)
    logits = jnp.dot(
        gathered,
        lax.all_gather(head, ROW_AXES, axis=0, tiled=True),
        preferred_element_type=jnp.float32,
    )
    row_peak = jnp.max(logits, axis=1)
    weights = jnp.exp(logits - row_peak[:, None])
    row_mass = jnp.sum(weights, axis=1)
    moment = jnp.sum(weights * logits, axis=1)
    column = targets - first_col
    columns = lax.broadcasted_iota(jnp.int32, logits.shape, 1)
    picked = jnp.sum(jnp.where(columns == column[:, None], logits, jnp.zeros_like(logits)), axis=1)

    stats = jnp.stack([row_peak, row_mass, moment, picked])
    every = lax.all_gather(stats, VOCAB_AXES, axis=0, tiled=False)
    peaks = every[:, 0]
    highest = jnp.max(peaks, axis=0)
    factor = jnp.exp(peaks - highest[None, :])
    mass_all = jnp.sum(every[:, 1] * factor, axis=0)
    moment_all = jnp.sum(every[:, 2] * factor, axis=0)
    picked_all = jnp.sum(every[:, 3], axis=0)
    block_target = jnp.where(targets >= block_first, picked_all, prior_target)
    logprob, entropy = finish_rows(
        highest, mass_all, moment_all, block_target, live, prior_lse, prior_mean
    )

    share = rows_here // spread
    begin = which * share
    logprob_share = lax.dynamic_slice_in_dim(logprob, begin, share, 0)
    entropy_share = lax.dynamic_slice_in_dim(entropy, begin, share, 0)

    global_rows = lax.axis_index(ROW_AXES) * rows_here + jnp.arange(rows_here, dtype=jnp.int32)
    endings = jnp.cumsum(seq_lengths)
    member = jnp.sum((global_rows[:, None] >= endings[None, :]).astype(jnp.int32), axis=1)
    onehot = (member[:, None] == jnp.arange(SEQS, dtype=jnp.int32)[None, :]).astype(jnp.float32)
    partial_sums = jnp.sum(onehot * logprob[:, None], axis=0)
    sums = lax.psum(lax.psum(partial_sums, "x"), "y")
    seq_mean = sums / seq_lengths.astype(jnp.float32)
    grouped = seq_mean.reshape(SEQS // GSIZE, GSIZE)
    seq_score = (grouped - jnp.mean(grouped, axis=1, keepdims=True)).reshape(SEQS)
    return (logprob_share, entropy_share, seq_score)


def solution(mesh):
    rows_y = 8 if mesh.shape["rows"] % 8 == 0 else 1
    vocab_c = 2 if mesh.shape["vocab"] % 2 == 0 else 1
    devices = mesh.devices.reshape(
        rows_y, mesh.shape["rows"] // rows_y, mesh.shape["vocab"] // vocab_c, vocab_c
    )
    fine = jax.sharding.Mesh(devices, ("y", "x", "z", "c"))
    rows, vocab = ROW_AXES, VOCAB_AXES
    return jax.shard_map(
        local,
        mesh=fine,
        in_specs=(
            P(rows, vocab),
            P(rows, vocab),
            P(rows),
            P(rows),
            P(rows),
            P(rows),
            P(rows),
            P(),
        ),
        out_specs=(P(rows + vocab), P(rows + vocab), P()),
        check_vma=False,
    )
```

```python
import jax
import jax.numpy as jnp
from jax import lax
from jax.sharding import PartitionSpec as P

VOCAB = 128256
SEQS = 32
GSIZE = 8
ROW_AXES = ("y", "x")
VOCAB_AXES = ("z", "c")


def finish_rows(block_peak, block_mass, block_moment, block_target, live, prior_lse, prior_mean):
    highest = jnp.maximum(block_peak, prior_lse)
    earlier = jnp.exp(prior_lse - highest)
    scaled = jnp.exp(block_peak - highest)
    total_mass = earlier + block_mass * scaled
    norm_log = highest + jnp.log(total_mass)
    average = (earlier * prior_mean + scaled * block_moment) / total_mass
    keeping = live.astype(jnp.float32)
    return (keeping * (block_target - norm_log), keeping * (norm_log - average))


def gather_hidden(hidden):
    nz = lax.axis_size("z")
    z = lax.axis_index("z")
    c = lax.axis_index("c")
    nc = lax.axis_size("c")
    width = hidden.shape[1]
    ahead = [(i, (i + 1) % nz) for i in range(nz)]
    behind = [(i, (i - 1) % nz) for i in range(nz)]
    across = [(i, (i + 1) % nc) for i in range(nc)]
    full = jnp.zeros((hidden.shape[0], width * nz * nc), hidden.dtype)

    def place(buf, piece, chip, core):
        slot = (chip * nc + core) * width
        return lax.dynamic_update_slice(buf, piece, (0, slot))

    def share(buf, piece, chip):
        buf = place(buf, piece, chip, c)
        if nc > 1:
            other = lax.ppermute(piece, "c", across)
            buf = place(buf, other, chip, (c + 1) % nc)
        return buf

    full = share(full, hidden, z)
    fwd = hidden
    bwd = hidden
    for step in range(1, nz // 2 + 1):
        fwd = lax.ppermute(fwd, "z", ahead)
        if step <= (nz - 1) // 2:
            bwd = lax.ppermute(bwd, "z", behind)
        full = share(full, fwd, (z - step) % nz)
        if step <= (nz - 1) // 2:
            full = share(full, bwd, (z + step) % nz)
    return full


def ring_gather(block, axis, place, buf):
    n = lax.axis_size(axis)
    me = lax.axis_index(axis)
    ahead = [(i, (i + 1) % n) for i in range(n)]
    behind = [(i, (i - 1) % n) for i in range(n)]
    buf = place(buf, block, me)
    fwd = block
    bwd = block
    for step in range(1, n // 2 + 1):
        fwd = lax.ppermute(fwd, axis, ahead)
        if step <= (n - 1) // 2:
            bwd = lax.ppermute(bwd, axis, behind)
        buf = place(buf, fwd, (me - step) % n)
        if step <= (n - 1) // 2:
            buf = place(buf, bwd, (me + step) % n)
    return buf


def gather_head_part(part):
    depth = part.shape[0]
    nx = lax.axis_size("x")
    ny = lax.axis_size("y")

    def put_x(buf, piece, index):
        return lax.dynamic_update_slice(buf, piece, (index * depth, 0))

    strip = ring_gather(part, "x", put_x, jnp.zeros((depth * nx, part.shape[1]), part.dtype))

    def put_y(buf, piece, index):
        return lax.dynamic_update_slice(buf, piece, (index * depth * nx, 0))

    return ring_gather(strip, "y", put_y, jnp.zeros((depth * nx * ny, part.shape[1]), part.dtype))


def local(hidden, head, targets, live, prior_lse, prior_mean, prior_target, seq_lengths):
    rows_here = hidden.shape[0]
    cols_here = head.shape[1]
    spread = lax.axis_size(VOCAB_AXES)
    which = lax.axis_index(VOCAB_AXES)
    block_first = VOCAB - cols_here * spread
    first_col = block_first + which * cols_here
    gathered = gather_hidden(hidden)
    split = (cols_here // 2) // 128 * 128
    head_sc = lax.all_gather(head[:, :split], ROW_AXES, axis=0, tiled=True)
    head_ring = gather_head_part(head[:, split:])
    logits = jnp.concatenate(
        [
            jnp.dot(gathered, head_sc, preferred_element_type=jnp.float32),
            jnp.dot(gathered, head_ring, preferred_element_type=jnp.float32),
        ],
        axis=1,
    )
    row_peak = jnp.max(logits, axis=1)
    weights = jnp.exp(logits - row_peak[:, None])
    row_mass = jnp.sum(weights, axis=1)
    moment = jnp.sum(weights * logits, axis=1)
    column = targets - first_col
    columns = lax.broadcasted_iota(jnp.int32, logits.shape, 1)
    picked = jnp.sum(jnp.where(columns == column[:, None], logits, jnp.zeros_like(logits)), axis=1)

    stats = jnp.stack([row_peak, row_mass, moment, picked])
    every = lax.all_gather(stats, VOCAB_AXES, axis=0, tiled=False)
    peaks = every[:, 0]
    highest = jnp.max(peaks, axis=0)
    factor = jnp.exp(peaks - highest[None, :])
    mass_all = jnp.sum(every[:, 1] * factor, axis=0)
    moment_all = jnp.sum(every[:, 2] * factor, axis=0)
    picked_all = jnp.sum(every[:, 3], axis=0)
    block_target = jnp.where(targets >= block_first, picked_all, prior_target)
    logprob, entropy = finish_rows(
        highest, mass_all, moment_all, block_target, live, prior_lse, prior_mean
    )

    share = rows_here // spread
    begin = which * share
    logprob_share = lax.dynamic_slice_in_dim(logprob, begin, share, 0)
    entropy_share = lax.dynamic_slice_in_dim(entropy, begin, share, 0)

    global_rows = lax.axis_index(ROW_AXES) * rows_here + jnp.arange(rows_here, dtype=jnp.int32)
    endings = jnp.cumsum(seq_lengths)
    member = jnp.sum((global_rows[:, None] >= endings[None, :]).astype(jnp.int32), axis=1)
    onehot = (member[:, None] == jnp.arange(SEQS, dtype=jnp.int32)[None, :]).astype(jnp.float32)
    partial_sums = jnp.sum(onehot * logprob[:, None], axis=0)
    sums = lax.psum(lax.psum(partial_sums, "x"), "y")
    seq_mean = sums / seq_lengths.astype(jnp.float32)
    grouped = seq_mean.reshape(SEQS // GSIZE, GSIZE)
    seq_score = (grouped - jnp.mean(grouped, axis=1, keepdims=True)).reshape(SEQS)
    return (logprob_share, entropy_share, seq_score)


def solution(mesh):
    rows_y = 8 if mesh.shape["rows"] % 8 == 0 else 1
    vocab_c = 2 if mesh.shape["vocab"] % 2 == 0 else 1
    devices = mesh.devices.reshape(
        rows_y, mesh.shape["rows"] // rows_y, mesh.shape["vocab"] // vocab_c, vocab_c
    )
    fine = jax.sharding.Mesh(devices, ("y", "x", "z", "c"))
    rows, vocab = ROW_AXES, VOCAB_AXES
    return jax.shard_map(
        local,
        mesh=fine,
        in_specs=(
            P(rows, vocab),
            P(rows, vocab),
            P(rows),
            P(rows),
            P(rows),
            P(rows),
            P(rows),
            P(),
        ),
        out_specs=(P(rows + vocab), P(rows + vocab), P()),
        check_vma=False,
    )
```

```python
import jax
import jax.numpy as jnp
from jax import lax
from jax.sharding import PartitionSpec as P

VOCAB = 128256
SEQS = 32
GSIZE = 8
ROW_AXES = ("y", "x")
VOCAB_AXES = ("z", "c")


def finish_rows(block_peak, block_mass, block_moment, block_target, live, prior_lse, prior_mean):
    highest = jnp.maximum(block_peak, prior_lse)
    earlier = jnp.exp(prior_lse - highest)
    scaled = jnp.exp(block_peak - highest)
    total_mass = earlier + block_mass * scaled
    norm_log = highest + jnp.log(total_mass)
    average = (earlier * prior_mean + scaled * block_moment) / total_mass
    keeping = live.astype(jnp.float32)
    return (keeping * (block_target - norm_log), keeping * (norm_log - average))


def gather_hidden(hidden):
    nz = lax.axis_size("z")
    z = lax.axis_index("z")
    c = lax.axis_index("c")
    nc = lax.axis_size("c")
    width = hidden.shape[1]
    ahead = [(i, (i + 1) % nz) for i in range(nz)]
    behind = [(i, (i - 1) % nz) for i in range(nz)]
    across = [(i, (i + 1) % nc) for i in range(nc)]
    full = jnp.zeros((hidden.shape[0], width * nz * nc), hidden.dtype)

    def place(buf, piece, chip, core):
        slot = (chip * nc + core) * width
        return lax.dynamic_update_slice(buf, piece, (0, slot))

    def share(buf, piece, chip):
        buf = place(buf, piece, chip, c)
        if nc > 1:
            other = lax.ppermute(piece, "c", across)
            buf = place(buf, other, chip, (c + 1) % nc)
        return buf

    full = share(full, hidden, z)
    fwd = hidden
    bwd = hidden
    for step in range(1, nz // 2 + 1):
        fwd = lax.ppermute(fwd, "z", ahead)
        if step <= (nz - 1) // 2:
            bwd = lax.ppermute(bwd, "z", behind)
        full = share(full, fwd, (z - step) % nz)
        if step <= (nz - 1) // 2:
            full = share(full, bwd, (z + step) % nz)
    return full


def ring_gather(block, axis, place, buf):
    n = lax.axis_size(axis)
    me = lax.axis_index(axis)
    ahead = [(i, (i + 1) % n) for i in range(n)]
    behind = [(i, (i - 1) % n) for i in range(n)]
    buf = place(buf, block, me)
    fwd = block
    bwd = block
    for step in range(1, n // 2 + 1):
        fwd = lax.ppermute(fwd, axis, ahead)
        if step <= (n - 1) // 2:
            bwd = lax.ppermute(bwd, axis, behind)
        buf = place(buf, fwd, (me - step) % n)
        if step <= (n - 1) // 2:
            buf = place(buf, bwd, (me + step) % n)
    return buf


def gather_head(head):
    depth, cols = head.shape
    nx = lax.axis_size("x")
    ny = lax.axis_size("y")
    half = (cols // 2) // 128 * 128

    def put_x(buf, piece, index):
        return lax.dynamic_update_slice(buf, piece, (index * depth, 0))

    def put_y(buf, piece, index):
        return lax.dynamic_update_slice(buf, piece, (index * depth * nx, 0))

    first = head[:, :half]
    strip = ring_gather(first, "x", put_x, jnp.zeros((depth * nx, half), head.dtype))
    first_full = ring_gather(strip, "y", put_y, jnp.zeros((depth * nx * ny, half), head.dtype))

    second = head[:, half:]
    width = cols - half

    def put_col(buf, piece, index):
        return lax.dynamic_update_slice(buf, piece[:, None], (0, index, 0, 0))

    def put_row(buf, piece, index):
        return lax.dynamic_update_slice(buf, piece[None], (index, 0, 0))

    column = ring_gather(second, "y", put_row, jnp.zeros((ny, depth, width), head.dtype))
    second_full = ring_gather(column, "x", put_col, jnp.zeros((ny, nx, depth, width), head.dtype))
    return first_full, second_full.reshape(ny * nx * depth, width)


def local(hidden, head, targets, live, prior_lse, prior_mean, prior_target, seq_lengths):
    rows_here = hidden.shape[0]
    cols_here = head.shape[1]
    spread = lax.axis_size(VOCAB_AXES)
    which = lax.axis_index(VOCAB_AXES)
    block_first = VOCAB - cols_here * spread
    first_col = block_first + which * cols_here
    gathered = lax.all_gather(hidden, VOCAB_AXES, axis=1, tiled=True)
    head_first, head_second = gather_head(head)
    logits = jnp.concatenate(
        [
            jnp.dot(gathered, head_first, preferred_element_type=jnp.float32),
            jnp.dot(gathered, head_second, preferred_element_type=jnp.float32),
        ],
        axis=1,
    )
    row_peak = jnp.max(logits, axis=1)
    weights = jnp.exp(logits - row_peak[:, None])
    row_mass = jnp.sum(weights, axis=1)
    moment = jnp.sum(weights * logits, axis=1)
    column = targets - first_col
    columns = lax.broadcasted_iota(jnp.int32, logits.shape, 1)
    picked = jnp.sum(jnp.where(columns == column[:, None], logits, jnp.zeros_like(logits)), axis=1)

    stats = jnp.stack([row_peak, row_mass, moment, picked])
    every = lax.all_gather(stats, VOCAB_AXES, axis=0, tiled=False)
    peaks = every[:, 0]
    highest = jnp.max(peaks, axis=0)
    factor = jnp.exp(peaks - highest[None, :])
    mass_all = jnp.sum(every[:, 1] * factor, axis=0)
    moment_all = jnp.sum(every[:, 2] * factor, axis=0)
    picked_all = jnp.sum(every[:, 3], axis=0)
    block_target = jnp.where(targets >= block_first, picked_all, prior_target)
    logprob, entropy = finish_rows(
        highest, mass_all, moment_all, block_target, live, prior_lse, prior_mean
    )

    share = rows_here // spread
    begin = which * share
    logprob_share = lax.dynamic_slice_in_dim(logprob, begin, share, 0)
    entropy_share = lax.dynamic_slice_in_dim(entropy, begin, share, 0)

    global_rows = lax.axis_index(ROW_AXES) * rows_here + jnp.arange(rows_here, dtype=jnp.int32)
    endings = jnp.cumsum(seq_lengths)
    member = jnp.sum((global_rows[:, None] >= endings[None, :]).astype(jnp.int32), axis=1)
    onehot = (member[:, None] == jnp.arange(SEQS, dtype=jnp.int32)[None, :]).astype(jnp.float32)
    partial_sums = jnp.sum(onehot * logprob[:, None], axis=0)
    sums = lax.psum(lax.psum(partial_sums, "x"), "y")
    seq_mean = sums / seq_lengths.astype(jnp.float32)
    grouped = seq_mean.reshape(SEQS // GSIZE, GSIZE)
    seq_score = (grouped - jnp.mean(grouped, axis=1, keepdims=True)).reshape(SEQS)
    return (logprob_share, entropy_share, seq_score)


def solution(mesh):
    rows_y = 8 if mesh.shape["rows"] % 8 == 0 else 1
    vocab_c = 2 if mesh.shape["vocab"] % 2 == 0 else 1
    devices = mesh.devices.reshape(
        rows_y, mesh.shape["rows"] // rows_y, mesh.shape["vocab"] // vocab_c, vocab_c
    )
    fine = jax.sharding.Mesh(devices, ("y", "x", "z", "c"))
    rows, vocab = ROW_AXES, VOCAB_AXES
    return jax.shard_map(
        local,
        mesh=fine,
        in_specs=(
            P(rows, vocab),
            P(rows, vocab),
            P(rows),
            P(rows),
            P(rows),
            P(rows),
            P(rows),
            P(),
        ),
        out_specs=(P(rows + vocab), P(rows + vocab), P()),
        check_vma=False,
    )
```

```python
import jax
import jax.numpy as jnp
from jax import lax
from jax.sharding import PartitionSpec as P

VOCAB = 128256
SEQS = 32
GSIZE = 8
ROW_AXES = ("y", "x")
VOCAB_AXES = ("z", "c")


def finish_rows(block_peak, block_mass, block_moment, block_target, live, prior_lse, prior_mean):
    highest = jnp.maximum(block_peak, prior_lse)
    earlier = jnp.exp(prior_lse - highest)
    scaled = jnp.exp(block_peak - highest)
    total_mass = earlier + block_mass * scaled
    norm_log = highest + jnp.log(total_mass)
    average = (earlier * prior_mean + scaled * block_moment) / total_mass
    keeping = live.astype(jnp.float32)
    return (keeping * (block_target - norm_log), keeping * (norm_log - average))


def gather_hidden(hidden):
    nz = lax.axis_size("z")
    z = lax.axis_index("z")
    c = lax.axis_index("c")
    nc = lax.axis_size("c")
    width = hidden.shape[1]
    ahead = [(i, (i + 1) % nz) for i in range(nz)]
    behind = [(i, (i - 1) % nz) for i in range(nz)]
    across = [(i, (i + 1) % nc) for i in range(nc)]
    full = jnp.zeros((hidden.shape[0], width * nz * nc), hidden.dtype)

    def place(buf, piece, chip, core):
        slot = (chip * nc + core) * width
        return lax.dynamic_update_slice(buf, piece, (0, slot))

    def share(buf, piece, chip):
        buf = place(buf, piece, chip, c)
        if nc > 1:
            other = lax.ppermute(piece, "c", across)
            buf = place(buf, other, chip, (c + 1) % nc)
        return buf

    full = share(full, hidden, z)
    fwd = hidden
    bwd = hidden
    for step in range(1, nz // 2 + 1):
        fwd = lax.ppermute(fwd, "z", ahead)
        if step <= (nz - 1) // 2:
            bwd = lax.ppermute(bwd, "z", behind)
        full = share(full, fwd, (z - step) % nz)
        if step <= (nz - 1) // 2:
            full = share(full, bwd, (z + step) % nz)
    return full


def local(hidden, head, targets, live, prior_lse, prior_mean, prior_target, seq_lengths):
    rows_here = hidden.shape[0]
    cols_here = head.shape[1]
    spread = lax.axis_size(VOCAB_AXES)
    which = lax.axis_index(VOCAB_AXES)
    block_first = VOCAB - cols_here * spread
    first_col = block_first + which * cols_here
    gathered = gather_hidden(hidden)
    logits = jnp.dot(
        gathered,
        lax.all_gather(lax.all_gather(head, "x", axis=0, tiled=True), "y", axis=0, tiled=True),
        preferred_element_type=jnp.float32,
    )
    row_peak = jnp.max(logits, axis=1)
    weights = jnp.exp(logits - row_peak[:, None])
    row_mass = jnp.sum(weights, axis=1)
    moment = jnp.sum(weights * logits, axis=1)
    column = targets - first_col
    columns = lax.broadcasted_iota(jnp.int32, logits.shape, 1)
    picked = jnp.sum(jnp.where(columns == column[:, None], logits, jnp.zeros_like(logits)), axis=1)

    stats = jnp.stack([row_peak, row_mass, moment, picked])
    every = lax.all_gather(stats, VOCAB_AXES, axis=0, tiled=False)
    peaks = every[:, 0]
    highest = jnp.max(peaks, axis=0)
    factor = jnp.exp(peaks - highest[None, :])
    mass_all = jnp.sum(every[:, 1] * factor, axis=0)
    moment_all = jnp.sum(every[:, 2] * factor, axis=0)
    picked_all = jnp.sum(every[:, 3], axis=0)
    block_target = jnp.where(targets >= block_first, picked_all, prior_target)
    logprob, entropy = finish_rows(
        highest, mass_all, moment_all, block_target, live, prior_lse, prior_mean
    )

    share = rows_here // spread
    begin = which * share
    logprob_share = lax.dynamic_slice_in_dim(logprob, begin, share, 0)
    entropy_share = lax.dynamic_slice_in_dim(entropy, begin, share, 0)

    global_rows = lax.axis_index(ROW_AXES) * rows_here + jnp.arange(rows_here, dtype=jnp.int32)
    endings = jnp.cumsum(seq_lengths)
    member = jnp.sum((global_rows[:, None] >= endings[None, :]).astype(jnp.int32), axis=1)
    onehot = (member[:, None] == jnp.arange(SEQS, dtype=jnp.int32)[None, :]).astype(jnp.float32)
    partial_sums = jnp.sum(onehot * logprob[:, None], axis=0)
    sums = lax.psum(lax.psum(partial_sums, "x"), "y")
    seq_mean = sums / seq_lengths.astype(jnp.float32)
    grouped = seq_mean.reshape(SEQS // GSIZE, GSIZE)
    seq_score = (grouped - jnp.mean(grouped, axis=1, keepdims=True)).reshape(SEQS)
    return (logprob_share, entropy_share, seq_score)


def solution(mesh):
    rows_y = 8 if mesh.shape["rows"] % 8 == 0 else 1
    vocab_c = 2 if mesh.shape["vocab"] % 2 == 0 else 1
    devices = mesh.devices.reshape(
        rows_y, mesh.shape["rows"] // rows_y, mesh.shape["vocab"] // vocab_c, vocab_c
    )
    fine = jax.sharding.Mesh(devices, ("y", "x", "z", "c"))
    rows, vocab = ROW_AXES, VOCAB_AXES
    return jax.shard_map(
        local,
        mesh=fine,
        in_specs=(
            P(rows, vocab),
            P(rows, vocab),
            P(rows),
            P(rows),
            P(rows),
            P(rows),
            P(rows),
            P(),
        ),
        out_specs=(P(rows + vocab), P(rows + vocab), P()),
        check_vma=False,
    )
```

```python
import jax
import jax.numpy as jnp
from jax import lax
from jax.sharding import PartitionSpec as P

VOCAB = 128256
SEQS = 32
GSIZE = 8
ROW_AXES = ("y", "x")
VOCAB_AXES = ("z", "c")


def finish_rows(block_peak, block_mass, block_moment, block_target, live, prior_lse, prior_mean):
    highest = jnp.maximum(block_peak, prior_lse)
    earlier = jnp.exp(prior_lse - highest)
    scaled = jnp.exp(block_peak - highest)
    total_mass = earlier + block_mass * scaled
    norm_log = highest + jnp.log(total_mass)
    average = (earlier * prior_mean + scaled * block_moment) / total_mass
    keeping = live.astype(jnp.float32)
    return (keeping * (block_target - norm_log), keeping * (norm_log - average))


def gather_hidden(hidden):
    nz = lax.axis_size("z")
    z = lax.axis_index("z")
    c = lax.axis_index("c")
    nc = lax.axis_size("c")
    width = hidden.shape[1]
    ahead = [(i, (i + 1) % nz) for i in range(nz)]
    behind = [(i, (i - 1) % nz) for i in range(nz)]
    across = [(i, (i + 1) % nc) for i in range(nc)]
    full = jnp.zeros((hidden.shape[0], width * nz * nc), hidden.dtype)

    def place(buf, piece, chip, core):
        slot = (chip * nc + core) * width
        return lax.dynamic_update_slice(buf, piece, (0, slot))

    def share(buf, piece, chip):
        buf = place(buf, piece, chip, c)
        if nc > 1:
            other = lax.ppermute(piece, "c", across)
            buf = place(buf, other, chip, (c + 1) % nc)
        return buf

    full = share(full, hidden, z)
    fwd = hidden
    bwd = hidden
    for step in range(1, nz // 2 + 1):
        fwd = lax.ppermute(fwd, "z", ahead)
        if step <= (nz - 1) // 2:
            bwd = lax.ppermute(bwd, "z", behind)
        full = share(full, fwd, (z - step) % nz)
        if step <= (nz - 1) // 2:
            full = share(full, bwd, (z + step) % nz)
    return full


def butterfly_sum(value, axis):
    n = lax.axis_size(axis)
    step = 1
    while step < n:
        value = value + lax.ppermute(value, axis, [(i, i ^ step) for i in range(n)])
        step *= 2
    return value


def local(hidden, head, targets, live, prior_lse, prior_mean, prior_target, seq_lengths):
    rows_here = hidden.shape[0]
    cols_here = head.shape[1]
    spread = lax.axis_size(VOCAB_AXES)
    which = lax.axis_index(VOCAB_AXES)
    block_first = VOCAB - cols_here * spread
    first_col = block_first + which * cols_here
    gathered = gather_hidden(hidden)
    logits = jnp.dot(
        gathered,
        lax.all_gather(head, ROW_AXES, axis=0, tiled=True),
        preferred_element_type=jnp.float32,
    )
    row_peak = jnp.max(logits, axis=1)
    weights = jnp.exp(logits - row_peak[:, None])
    row_mass = jnp.sum(weights, axis=1)
    moment = jnp.sum(weights * logits, axis=1)
    column = targets - first_col
    columns = lax.broadcasted_iota(jnp.int32, logits.shape, 1)
    picked = jnp.sum(jnp.where(columns == column[:, None], logits, jnp.zeros_like(logits)), axis=1)

    stats = jnp.stack([row_peak, row_mass, moment, picked])
    slots = jnp.zeros((spread,) + stats.shape, stats.dtype)
    every = lax.dynamic_update_slice(slots, stats[None], (which, 0, 0))
    every = butterfly_sum(butterfly_sum(every, "c"), "z")
    peaks = every[:, 0]
    highest = jnp.max(peaks, axis=0)
    factor = jnp.exp(peaks - highest[None, :])
    mass_all = jnp.sum(every[:, 1] * factor, axis=0)
    moment_all = jnp.sum(every[:, 2] * factor, axis=0)
    picked_all = jnp.sum(every[:, 3], axis=0)
    block_target = jnp.where(targets >= block_first, picked_all, prior_target)
    logprob, entropy = finish_rows(
        highest, mass_all, moment_all, block_target, live, prior_lse, prior_mean
    )

    share = rows_here // spread
    begin = which * share
    logprob_share = lax.dynamic_slice_in_dim(logprob, begin, share, 0)
    entropy_share = lax.dynamic_slice_in_dim(entropy, begin, share, 0)

    global_rows = lax.axis_index(ROW_AXES) * rows_here + jnp.arange(rows_here, dtype=jnp.int32)
    endings = jnp.cumsum(seq_lengths)
    member = jnp.sum((global_rows[:, None] >= endings[None, :]).astype(jnp.int32), axis=1)
    onehot = (member[:, None] == jnp.arange(SEQS, dtype=jnp.int32)[None, :]).astype(jnp.float32)
    partial_sums = jnp.sum(onehot * logprob[:, None], axis=0)
    sums = butterfly_sum(butterfly_sum(partial_sums, "x"), "y")
    seq_mean = sums / seq_lengths.astype(jnp.float32)
    grouped = seq_mean.reshape(SEQS // GSIZE, GSIZE)
    seq_score = (grouped - jnp.mean(grouped, axis=1, keepdims=True)).reshape(SEQS)
    return (logprob_share, entropy_share, seq_score)


def solution(mesh):
    rows_y = 8 if mesh.shape["rows"] % 8 == 0 else 1
    vocab_c = 2 if mesh.shape["vocab"] % 2 == 0 else 1
    devices = mesh.devices.reshape(
        rows_y, mesh.shape["rows"] // rows_y, mesh.shape["vocab"] // vocab_c, vocab_c
    )
    fine = jax.sharding.Mesh(devices, ("y", "x", "z", "c"))
    rows, vocab = ROW_AXES, VOCAB_AXES
    return jax.shard_map(
        local,
        mesh=fine,
        in_specs=(
            P(rows, vocab),
            P(rows, vocab),
            P(rows),
            P(rows),
            P(rows),
            P(rows),
            P(rows),
            P(),
        ),
        out_specs=(P(rows + vocab), P(rows + vocab), P()),
        check_vma=False,
    )
```

```python
import jax
import jax.numpy as jnp
from jax import lax
from jax.sharding import PartitionSpec as P

VOCAB = 128256
SEQS = 32
GSIZE = 8
ROW_AXES = ("y", "x")
VOCAB_AXES = ("z", "c")


def finish_rows(block_peak, block_mass, block_moment, block_target, live, prior_lse, prior_mean):
    highest = jnp.maximum(block_peak, prior_lse)
    earlier = jnp.exp(prior_lse - highest)
    scaled = jnp.exp(block_peak - highest)
    total_mass = earlier + block_mass * scaled
    norm_log = highest + jnp.log(total_mass)
    average = (earlier * prior_mean + scaled * block_moment) / total_mass
    keeping = live.astype(jnp.float32)
    return (keeping * (block_target - norm_log), keeping * (norm_log - average))


def gather_hidden(hidden):
    nz = lax.axis_size("z")
    z = lax.axis_index("z")
    c = lax.axis_index("c")
    nc = lax.axis_size("c")
    width = hidden.shape[1]
    ahead = [(i, (i + 1) % nz) for i in range(nz)]
    behind = [(i, (i - 1) % nz) for i in range(nz)]
    across = [(i, (i + 1) % nc) for i in range(nc)]
    full = jnp.zeros((hidden.shape[0], width * nz * nc), hidden.dtype)

    def place(buf, piece, chip, core):
        slot = (chip * nc + core) * width
        return lax.dynamic_update_slice(buf, piece, (0, slot))

    def share(buf, piece, chip):
        buf = place(buf, piece, chip, c)
        if nc > 1:
            other = lax.ppermute(piece, "c", across)
            buf = place(buf, other, chip, (c + 1) % nc)
        return buf

    full = share(full, hidden, z)
    fwd = hidden
    bwd = hidden
    for step in range(1, nz // 2 + 1):
        fwd = lax.ppermute(fwd, "z", ahead)
        if step <= (nz - 1) // 2:
            bwd = lax.ppermute(bwd, "z", behind)
        full = share(full, fwd, (z - step) % nz)
        if step <= (nz - 1) // 2:
            full = share(full, bwd, (z + step) % nz)
    return full


def local(hidden, head, targets, live, prior_lse, prior_mean, prior_target, seq_lengths):
    rows_here = hidden.shape[0]
    cols_here = head.shape[1]
    spread = lax.axis_size(VOCAB_AXES)
    which = lax.axis_index(VOCAB_AXES)
    block_first = VOCAB - cols_here * spread
    first_col = block_first + which * cols_here
    gathered = gather_hidden(hidden)
    logits = jnp.dot(
        gathered,
        lax.all_gather(head, ROW_AXES, axis=0, tiled=True),
        preferred_element_type=jnp.float32,
    )
    row_peak = jnp.max(logits, axis=1)
    weights = jnp.exp(logits - row_peak[:, None])
    row_mass = jnp.sum(weights, axis=1)
    moment = jnp.sum(weights * logits, axis=1)
    column = targets - first_col
    columns = lax.broadcasted_iota(jnp.int32, logits.shape, 1)
    picked = jnp.sum(jnp.where(columns == column[:, None], logits, jnp.zeros_like(logits)), axis=1)

    stats = jnp.stack([row_peak, row_mass, moment, picked])
    copies = jnp.broadcast_to(stats[None], (spread,) + stats.shape)
    every = lax.all_to_all(copies, VOCAB_AXES, 0, 0, tiled=True)
    peaks = every[:, 0]
    highest = jnp.max(peaks, axis=0)
    factor = jnp.exp(peaks - highest[None, :])
    mass_all = jnp.sum(every[:, 1] * factor, axis=0)
    moment_all = jnp.sum(every[:, 2] * factor, axis=0)
    picked_all = jnp.sum(every[:, 3], axis=0)
    block_target = jnp.where(targets >= block_first, picked_all, prior_target)
    logprob, entropy = finish_rows(
        highest, mass_all, moment_all, block_target, live, prior_lse, prior_mean
    )

    share = rows_here // spread
    begin = which * share
    logprob_share = lax.dynamic_slice_in_dim(logprob, begin, share, 0)
    entropy_share = lax.dynamic_slice_in_dim(entropy, begin, share, 0)

    global_rows = lax.axis_index(ROW_AXES) * rows_here + jnp.arange(rows_here, dtype=jnp.int32)
    endings = jnp.cumsum(seq_lengths)
    member = jnp.sum((global_rows[:, None] >= endings[None, :]).astype(jnp.int32), axis=1)
    onehot = (member[:, None] == jnp.arange(SEQS, dtype=jnp.int32)[None, :]).astype(jnp.float32)
    partial_sums = jnp.sum(onehot * logprob[:, None], axis=0)
    peers = lax.axis_size(ROW_AXES)
    spread_sums = jnp.broadcast_to(partial_sums[None], (peers, SEQS))
    sums = jnp.sum(lax.all_to_all(spread_sums, ROW_AXES, 0, 0, tiled=True), axis=0)
    seq_mean = sums / seq_lengths.astype(jnp.float32)
    grouped = seq_mean.reshape(SEQS // GSIZE, GSIZE)
    seq_score = (grouped - jnp.mean(grouped, axis=1, keepdims=True)).reshape(SEQS)
    return (logprob_share, entropy_share, seq_score)


def solution(mesh):
    rows_y = 8 if mesh.shape["rows"] % 8 == 0 else 1
    vocab_c = 2 if mesh.shape["vocab"] % 2 == 0 else 1
    devices = mesh.devices.reshape(
        rows_y, mesh.shape["rows"] // rows_y, mesh.shape["vocab"] // vocab_c, vocab_c
    )
    fine = jax.sharding.Mesh(devices, ("y", "x", "z", "c"))
    rows, vocab = ROW_AXES, VOCAB_AXES
    return jax.shard_map(
        local,
        mesh=fine,
        in_specs=(
            P(rows, vocab),
            P(rows, vocab),
            P(rows),
            P(rows),
            P(rows),
            P(rows),
            P(rows),
            P(),
        ),
        out_specs=(P(rows + vocab), P(rows + vocab), P()),
        check_vma=False,
    )
```

```python
import jax
import jax.numpy as jnp
from jax import lax
from jax.sharding import PartitionSpec as P

VOCAB = 128256
SEQS = 32
GSIZE = 8
ROW_AXES = ("y", "x")
VOCAB_AXES = ("z", "c")


def finish_rows(block_peak, block_mass, block_moment, block_target, live, prior_lse, prior_mean):
    highest = jnp.maximum(block_peak, prior_lse)
    earlier = jnp.exp(prior_lse - highest)
    scaled = jnp.exp(block_peak - highest)
    total_mass = earlier + block_mass * scaled
    norm_log = highest + jnp.log(total_mass)
    average = (earlier * prior_mean + scaled * block_moment) / total_mass
    keeping = live.astype(jnp.float32)
    return (keeping * (block_target - norm_log), keeping * (norm_log - average))


def gather_hidden(hidden):
    nz = lax.axis_size("z")
    z = lax.axis_index("z")
    c = lax.axis_index("c")
    nc = lax.axis_size("c")
    width = hidden.shape[1]
    ahead = [(i, (i + 1) % nz) for i in range(nz)]
    behind = [(i, (i - 1) % nz) for i in range(nz)]
    across = [(i, (i + 1) % nc) for i in range(nc)]
    full = jnp.zeros((hidden.shape[0], width * nz * nc), hidden.dtype)

    def place(buf, piece, chip, core):
        slot = (chip * nc + core) * width
        return lax.dynamic_update_slice(buf, piece, (0, slot))

    def share(buf, piece, chip):
        buf = place(buf, piece, chip, c)
        if nc > 1:
            other = lax.ppermute(piece, "c", across)
            buf = place(buf, other, chip, (c + 1) % nc)
        return buf

    full = share(full, hidden, z)
    fwd = hidden
    bwd = hidden
    for step in range(1, nz // 2 + 1):
        fwd = lax.ppermute(fwd, "z", ahead)
        if step <= (nz - 1) // 2:
            bwd = lax.ppermute(bwd, "z", behind)
        full = share(full, fwd, (z - step) % nz)
        if step <= (nz - 1) // 2:
            full = share(full, bwd, (z + step) % nz)
    return full


def local(hidden, head, targets, live, prior_lse, prior_mean, prior_target, seq_lengths):
    rows_here = hidden.shape[0]
    cols_here = head.shape[1]
    spread = lax.axis_size(VOCAB_AXES)
    which = lax.axis_index(VOCAB_AXES)
    block_first = VOCAB - cols_here * spread
    first_col = block_first + which * cols_here
    gathered = gather_hidden(hidden)
    logits = jnp.dot(
        gathered,
        lax.all_gather(head, ROW_AXES, axis=0, tiled=True),
        preferred_element_type=jnp.float32,
    )
    row_peak = jnp.max(logits, axis=1)
    weights = jnp.exp(logits - row_peak[:, None])
    row_mass = jnp.sum(weights, axis=1)
    moment = jnp.sum(weights * logits, axis=1)
    column = targets - first_col
    columns = lax.broadcasted_iota(jnp.int32, logits.shape, 1)
    picked = jnp.sum(jnp.where(columns == column[:, None], logits, jnp.zeros_like(logits)), axis=1)

    share = rows_here // spread
    begin = which * share
    inputs = jnp.stack(
        [
            prior_lse,
            prior_mean,
            prior_target,
            live.astype(jnp.float32),
            (targets >= block_first).astype(jnp.float32),
        ]
    )
    mine = lax.dynamic_slice_in_dim(inputs, begin, share, 1)
    stats = jnp.stack([row_peak, row_mass, moment, picked])
    payload = jnp.concatenate([stats.reshape(-1), mine.reshape(-1)])
    groups = lax.axis_size(ROW_AXES)
    everyone = groups * spread
    got = lax.all_to_all(
        jnp.broadcast_to(payload[None], (everyone, payload.shape[0])),
        ROW_AXES + VOCAB_AXES,
        0,
        0,
        tiled=True,
    ).reshape(groups, spread, payload.shape[0])
    every = got[:, :, : stats.size].reshape(groups, spread, 4, rows_here)
    rows_in = (
        got[:, :, stats.size :]
        .reshape(groups, spread, 5, share)
        .transpose(0, 2, 1, 3)
        .reshape(groups, 5, rows_here)
    )
    peaks = every[:, :, 0]
    highest = jnp.max(peaks, axis=1)
    factor = jnp.exp(peaks - highest[:, None, :])
    mass_all = jnp.sum(every[:, :, 1] * factor, axis=1)
    moment_all = jnp.sum(every[:, :, 2] * factor, axis=1)
    picked_all = jnp.sum(every[:, :, 3], axis=1)
    block_target = jnp.where(rows_in[:, 4] > 0.5, picked_all, rows_in[:, 2])
    logprob, entropy = finish_rows(
        highest, mass_all, moment_all, block_target, rows_in[:, 3], rows_in[:, 0], rows_in[:, 1]
    )
    group = lax.axis_index(ROW_AXES)
    logprob_share = lax.dynamic_slice(logprob, (group, begin), (1, share)).reshape(share)
    entropy_share = lax.dynamic_slice(entropy, (group, begin), (1, share)).reshape(share)

    all_rows = jnp.arange(groups * rows_here, dtype=jnp.int32)
    endings = jnp.cumsum(seq_lengths)
    member = jnp.sum((all_rows[:, None] >= endings[None, :]).astype(jnp.int32), axis=1)
    onehot = (member[:, None] == jnp.arange(SEQS, dtype=jnp.int32)[None, :]).astype(jnp.float32)
    sums = jnp.sum(onehot * logprob.reshape(-1)[:, None], axis=0)
    seq_mean = sums / seq_lengths.astype(jnp.float32)
    grouped = seq_mean.reshape(SEQS // GSIZE, GSIZE)
    seq_score = (grouped - jnp.mean(grouped, axis=1, keepdims=True)).reshape(SEQS)
    return (logprob_share, entropy_share, seq_score)


def solution(mesh):
    rows_y = 8 if mesh.shape["rows"] % 8 == 0 else 1
    vocab_c = 2 if mesh.shape["vocab"] % 2 == 0 else 1
    devices = mesh.devices.reshape(
        rows_y, mesh.shape["rows"] // rows_y, mesh.shape["vocab"] // vocab_c, vocab_c
    )
    fine = jax.sharding.Mesh(devices, ("y", "x", "z", "c"))
    rows, vocab = ROW_AXES, VOCAB_AXES
    return jax.shard_map(
        local,
        mesh=fine,
        in_specs=(
            P(rows, vocab),
            P(rows, vocab),
            P(rows),
            P(rows),
            P(rows),
            P(rows),
            P(rows),
            P(),
        ),
        out_specs=(P(rows + vocab), P(rows + vocab), P()),
        check_vma=False,
    )
```

```python
import jax
import jax.numpy as jnp
from jax import lax
from jax.sharding import PartitionSpec as P

VOCAB = 128256
SEQS = 32
GSIZE = 8
ROW_AXES = ("y", "x")
VOCAB_AXES = ("z", "c")


def finish_rows(block_peak, block_mass, block_moment, block_target, live, prior_lse, prior_mean):
    highest = jnp.maximum(block_peak, prior_lse)
    earlier = jnp.exp(prior_lse - highest)
    scaled = jnp.exp(block_peak - highest)
    total_mass = earlier + block_mass * scaled
    norm_log = highest + jnp.log(total_mass)
    average = (earlier * prior_mean + scaled * block_moment) / total_mass
    keeping = live.astype(jnp.float32)
    return (keeping * (block_target - norm_log), keeping * (norm_log - average))


def gather_hidden(hidden):
    nz = lax.axis_size("z")
    z = lax.axis_index("z")
    c = lax.axis_index("c")
    nc = lax.axis_size("c")
    width = hidden.shape[1]
    ahead = [(i, (i + 1) % nz) for i in range(nz)]
    behind = [(i, (i - 1) % nz) for i in range(nz)]
    across = [(i, (i + 1) % nc) for i in range(nc)]
    full = jnp.zeros((hidden.shape[0], width * nz * nc), hidden.dtype)

    def place(buf, piece, chip, core):
        slot = (chip * nc + core) * width
        return lax.dynamic_update_slice(buf, piece, (0, slot))

    def share(buf, piece, chip):
        buf = place(buf, piece, chip, c)
        if nc > 1:
            other = lax.ppermute(piece, "c", across)
            buf = place(buf, other, chip, (c + 1) % nc)
        return buf

    full = share(full, hidden, z)
    fwd = hidden
    bwd = hidden
    for step in range(1, nz // 2 + 1):
        fwd = lax.ppermute(fwd, "z", ahead)
        if step <= (nz - 1) // 2:
            bwd = lax.ppermute(bwd, "z", behind)
        full = share(full, fwd, (z - step) % nz)
        if step <= (nz - 1) // 2:
            full = share(full, bwd, (z + step) % nz)
    return full


def ring_gather(block, axis, place, buf):
    n = lax.axis_size(axis)
    me = lax.axis_index(axis)
    ahead = [(i, (i + 1) % n) for i in range(n)]
    behind = [(i, (i - 1) % n) for i in range(n)]
    buf = place(buf, block, me)
    fwd = block
    bwd = block
    for step in range(1, n // 2 + 1):
        fwd = lax.ppermute(fwd, axis, ahead)
        if step <= (n - 1) // 2:
            bwd = lax.ppermute(bwd, axis, behind)
        buf = place(buf, fwd, (me - step) % n)
        if step <= (n - 1) // 2:
            buf = place(buf, bwd, (me + step) % n)
    return buf


def spread_gather(block, axis):
    n = lax.axis_size(axis)
    return lax.all_to_all(jnp.broadcast_to(block[None], (n,) + block.shape), axis, 0, 0, tiled=True)


def gather_head(head):
    depth, cols = head.shape
    nx = lax.axis_size("x")
    ny = lax.axis_size("y")
    half = (cols // 2) // 128 * 128

    def put_y(buf, piece, index):
        return lax.dynamic_update_slice(buf, piece, (index * depth * nx, 0))

    strip = spread_gather(head[:, :half], "x").reshape(nx * depth, half)
    first_full = ring_gather(strip, "y", put_y, jnp.zeros((depth * nx * ny, half), head.dtype))

    width = cols - half

    def put_col(buf, piece, index):
        return lax.dynamic_update_slice(buf, piece[:, None], (0, index, 0, 0))

    column = spread_gather(head[:, half:], "y")
    second_full = ring_gather(column, "x", put_col, jnp.zeros((ny, nx, depth, width), head.dtype))
    return first_full, second_full.reshape(ny * nx * depth, width)


def local(hidden, head, targets, live, prior_lse, prior_mean, prior_target, seq_lengths):
    rows_here = hidden.shape[0]
    cols_here = head.shape[1]
    spread = lax.axis_size(VOCAB_AXES)
    which = lax.axis_index(VOCAB_AXES)
    block_first = VOCAB - cols_here * spread
    first_col = block_first + which * cols_here
    gathered = lax.all_gather(hidden, VOCAB_AXES, axis=1, tiled=True)
    head_first, head_second = gather_head(head)
    logits = jnp.concatenate(
        [
            jnp.dot(gathered, head_first, preferred_element_type=jnp.float32),
            jnp.dot(gathered, head_second, preferred_element_type=jnp.float32),
        ],
        axis=1,
    )
    row_peak = jnp.max(logits, axis=1)
    weights = jnp.exp(logits - row_peak[:, None])
    row_mass = jnp.sum(weights, axis=1)
    moment = jnp.sum(weights * logits, axis=1)
    column = targets - first_col
    columns = lax.broadcasted_iota(jnp.int32, logits.shape, 1)
    picked = jnp.sum(jnp.where(columns == column[:, None], logits, jnp.zeros_like(logits)), axis=1)

    stats = jnp.stack([row_peak, row_mass, moment, picked])
    copies = jnp.broadcast_to(stats[None], (spread,) + stats.shape)
    every = lax.all_to_all(copies, VOCAB_AXES, 0, 0, tiled=True)
    peaks = every[:, 0]
    highest = jnp.max(peaks, axis=0)
    factor = jnp.exp(peaks - highest[None, :])
    mass_all = jnp.sum(every[:, 1] * factor, axis=0)
    moment_all = jnp.sum(every[:, 2] * factor, axis=0)
    picked_all = jnp.sum(every[:, 3], axis=0)
    block_target = jnp.where(targets >= block_first, picked_all, prior_target)
    logprob, entropy = finish_rows(
        highest, mass_all, moment_all, block_target, live, prior_lse, prior_mean
    )

    share = rows_here // spread
    begin = which * share
    logprob_share = lax.dynamic_slice_in_dim(logprob, begin, share, 0)
    entropy_share = lax.dynamic_slice_in_dim(entropy, begin, share, 0)

    global_rows = lax.axis_index(ROW_AXES) * rows_here + jnp.arange(rows_here, dtype=jnp.int32)
    endings = jnp.cumsum(seq_lengths)
    member = jnp.sum((global_rows[:, None] >= endings[None, :]).astype(jnp.int32), axis=1)
    onehot = (member[:, None] == jnp.arange(SEQS, dtype=jnp.int32)[None, :]).astype(jnp.float32)
    partial_sums = jnp.sum(onehot * logprob[:, None], axis=0)
    peers = lax.axis_size(ROW_AXES)
    spread_sums = jnp.broadcast_to(partial_sums[None], (peers, SEQS))
    sums = jnp.sum(lax.all_to_all(spread_sums, ROW_AXES, 0, 0, tiled=True), axis=0)
    seq_mean = sums / seq_lengths.astype(jnp.float32)
    grouped = seq_mean.reshape(SEQS // GSIZE, GSIZE)
    seq_score = (grouped - jnp.mean(grouped, axis=1, keepdims=True)).reshape(SEQS)
    return (logprob_share, entropy_share, seq_score)


def solution(mesh):
    rows_y = 8 if mesh.shape["rows"] % 8 == 0 else 1
    vocab_c = 2 if mesh.shape["vocab"] % 2 == 0 else 1
    devices = mesh.devices.reshape(
        rows_y, mesh.shape["rows"] // rows_y, mesh.shape["vocab"] // vocab_c, vocab_c
    )
    fine = jax.sharding.Mesh(devices, ("y", "x", "z", "c"))
    rows, vocab = ROW_AXES, VOCAB_AXES
    return jax.shard_map(
        local,
        mesh=fine,
        in_specs=(
            P(rows, vocab),
            P(rows, vocab),
            P(rows),
            P(rows),
            P(rows),
            P(rows),
            P(rows),
            P(),
        ),
        out_specs=(P(rows + vocab), P(rows + vocab), P()),
        check_vma=False,
    )
```

```python
import jax
import jax.numpy as jnp
from jax import lax
from jax.experimental import pallas as pl
from jax.experimental.pallas import tpu as pltpu
from jax.sharding import PartitionSpec as P

VOCAB = 128256
SEQS = 32
GSIZE = 8
ROW_AXES = ("y", "x")
VOCAB_AXES = ("z", "c")


def finish_rows(block_peak, block_mass, block_moment, block_target, live, prior_lse, prior_mean):
    highest = jnp.maximum(block_peak, prior_lse)
    earlier = jnp.exp(prior_lse - highest)
    scaled = jnp.exp(block_peak - highest)
    total_mass = earlier + block_mass * scaled
    norm_log = highest + jnp.log(total_mass)
    average = (earlier * prior_mean + scaled * block_moment) / total_mass
    keeping = live.astype(jnp.float32)
    return (keeping * (block_target - norm_log), keeping * (norm_log - average))


def gather_hidden(hidden):
    nz = lax.axis_size("z")
    z = lax.axis_index("z")
    c = lax.axis_index("c")
    nc = lax.axis_size("c")
    width = hidden.shape[1]
    ahead = [(i, (i + 1) % nz) for i in range(nz)]
    behind = [(i, (i - 1) % nz) for i in range(nz)]
    across = [(i, (i + 1) % nc) for i in range(nc)]
    full = jnp.zeros((hidden.shape[0], width * nz * nc), hidden.dtype)

    def place(buf, piece, chip, core):
        slot = (chip * nc + core) * width
        return lax.dynamic_update_slice(buf, piece, (0, slot))

    def share(buf, piece, chip):
        buf = place(buf, piece, chip, c)
        if nc > 1:
            other = lax.ppermute(piece, "c", across)
            buf = place(buf, other, chip, (c + 1) % nc)
        return buf

    full = share(full, hidden, z)
    fwd = hidden
    bwd = hidden
    for step in range(1, nz // 2 + 1):
        fwd = lax.ppermute(fwd, "z", ahead)
        if step <= (nz - 1) // 2:
            bwd = lax.ppermute(bwd, "z", behind)
        full = share(full, fwd, (z - step) % nz)
        if step <= (nz - 1) // 2:
            full = share(full, bwd, (z + step) % nz)
    return full


def logits_kernel(h_ref, w_ref, o_ref, acc_ref):
    @pl.when(pl.program_id(0) == 0)
    def _():
        acc_ref[...] = jnp.zeros_like(acc_ref)

    acc_ref[...] += jnp.dot(h_ref[...], w_ref[...], preferred_element_type=jnp.float32)

    @pl.when(pl.program_id(0) == pl.num_programs(0) - 1)
    def _():
        o_ref[...] = acc_ref[...]


def logits_of(rows, head_full):
    m, k = rows.shape
    n = head_full.shape[1]
    depth = 2048 if k % 2048 == 0 else k
    return pl.pallas_call(
        logits_kernel,
        out_shape=jax.ShapeDtypeStruct((m, n), jnp.float32),
        grid=(k // depth,),
        in_specs=[
            pl.BlockSpec((m, depth), lambda i: (0, i)),
            pl.BlockSpec((depth, n), lambda i: (i, 0)),
        ],
        out_specs=pl.BlockSpec((m, n), lambda i: (0, 0)),
        scratch_shapes=[pltpu.VMEM((m, n), jnp.float32)],
        compiler_params=pltpu.CompilerParams(dimension_semantics=("arbitrary",)),
        cost_estimate=pl.CostEstimate(
            flops=2 * m * k * n, transcendentals=0, bytes_accessed=2 * (m * k + k * n) + 4 * m * n
        ),
    )(rows, head_full)


def local(hidden, head, targets, live, prior_lse, prior_mean, prior_target, seq_lengths):
    rows_here = hidden.shape[0]
    cols_here = head.shape[1]
    spread = lax.axis_size(VOCAB_AXES)
    which = lax.axis_index(VOCAB_AXES)
    block_first = VOCAB - cols_here * spread
    first_col = block_first + which * cols_here
    gathered = gather_hidden(hidden)
    logits = logits_of(gathered, lax.all_gather(head, ROW_AXES, axis=0, tiled=True))
    row_peak = jnp.max(logits, axis=1)
    weights = jnp.exp(logits - row_peak[:, None])
    row_mass = jnp.sum(weights, axis=1)
    moment = jnp.sum(weights * logits, axis=1)
    column = targets - first_col
    columns = lax.broadcasted_iota(jnp.int32, logits.shape, 1)
    picked = jnp.sum(jnp.where(columns == column[:, None], logits, jnp.zeros_like(logits)), axis=1)

    stats = jnp.stack([row_peak, row_mass, moment, picked])
    copies = jnp.broadcast_to(stats[None], (spread,) + stats.shape)
    every = lax.all_to_all(copies, VOCAB_AXES, 0, 0, tiled=True)
    peaks = every[:, 0]
    highest = jnp.max(peaks, axis=0)
    factor = jnp.exp(peaks - highest[None, :])
    mass_all = jnp.sum(every[:, 1] * factor, axis=0)
    moment_all = jnp.sum(every[:, 2] * factor, axis=0)
    picked_all = jnp.sum(every[:, 3], axis=0)
    block_target = jnp.where(targets >= block_first, picked_all, prior_target)
    logprob, entropy = finish_rows(
        highest, mass_all, moment_all, block_target, live, prior_lse, prior_mean
    )

    share = rows_here // spread
    begin = which * share
    logprob_share = lax.dynamic_slice_in_dim(logprob, begin, share, 0)
    entropy_share = lax.dynamic_slice_in_dim(entropy, begin, share, 0)

    global_rows = lax.axis_index(ROW_AXES) * rows_here + jnp.arange(rows_here, dtype=jnp.int32)
    endings = jnp.cumsum(seq_lengths)
    member = jnp.sum((global_rows[:, None] >= endings[None, :]).astype(jnp.int32), axis=1)
    onehot = (member[:, None] == jnp.arange(SEQS, dtype=jnp.int32)[None, :]).astype(jnp.float32)
    partial_sums = jnp.sum(onehot * logprob[:, None], axis=0)
    peers = lax.axis_size(ROW_AXES)
    spread_sums = jnp.broadcast_to(partial_sums[None], (peers, SEQS))
    sums = jnp.sum(lax.all_to_all(spread_sums, ROW_AXES, 0, 0, tiled=True), axis=0)
    seq_mean = sums / seq_lengths.astype(jnp.float32)
    grouped = seq_mean.reshape(SEQS // GSIZE, GSIZE)
    seq_score = (grouped - jnp.mean(grouped, axis=1, keepdims=True)).reshape(SEQS)
    return (logprob_share, entropy_share, seq_score)


def solution(mesh):
    rows_y = 8 if mesh.shape["rows"] % 8 == 0 else 1
    vocab_c = 2 if mesh.shape["vocab"] % 2 == 0 else 1
    devices = mesh.devices.reshape(
        rows_y, mesh.shape["rows"] // rows_y, mesh.shape["vocab"] // vocab_c, vocab_c
    )
    fine = jax.sharding.Mesh(devices, ("y", "x", "z", "c"))
    rows, vocab = ROW_AXES, VOCAB_AXES
    return jax.shard_map(
        local,
        mesh=fine,
        in_specs=(
            P(rows, vocab),
            P(rows, vocab),
            P(rows),
            P(rows),
            P(rows),
            P(rows),
            P(rows),
            P(),
        ),
        out_specs=(P(rows + vocab), P(rows + vocab), P()),
        check_vma=False,
    )
```

```python
import jax
import jax.numpy as jnp
from jax import lax
from jax.sharding import PartitionSpec as P

VOCAB = 128256
SEQS = 32
GSIZE = 8
ROW_AXES = ("y", "x")
VOCAB_AXES = ("z", "c")


def finish_rows(block_peak, block_mass, block_moment, block_target, live, prior_lse, prior_mean):
    highest = jnp.maximum(block_peak, prior_lse)
    earlier = jnp.exp(prior_lse - highest)
    scaled = jnp.exp(block_peak - highest)
    total_mass = earlier + block_mass * scaled
    norm_log = highest + jnp.log(total_mass)
    average = (earlier * prior_mean + scaled * block_moment) / total_mass
    keeping = live.astype(jnp.float32)
    return (keeping * (block_target - norm_log), keeping * (norm_log - average))


def gather_hidden(hidden):
    nz = lax.axis_size("z")
    z = lax.axis_index("z")
    c = lax.axis_index("c")
    nc = lax.axis_size("c")
    width = hidden.shape[1]
    ahead = [(i, (i + 1) % nz) for i in range(nz)]
    behind = [(i, (i - 1) % nz) for i in range(nz)]
    across = [(i, (i + 1) % nc) for i in range(nc)]
    full = jnp.zeros((hidden.shape[0], width * nz * nc), hidden.dtype)

    def place(buf, piece, chip, core):
        slot = (chip * nc + core) * width
        return lax.dynamic_update_slice(buf, piece, (0, slot))

    def share(buf, piece, chip):
        buf = place(buf, piece, chip, c)
        if nc > 1:
            other = lax.ppermute(piece, "c", across)
            buf = place(buf, other, chip, (c + 1) % nc)
        return buf

    full = share(full, hidden, z)
    fwd = hidden
    bwd = hidden
    for step in range(1, nz // 2 + 1):
        fwd = lax.ppermute(fwd, "z", ahead)
        if step <= (nz - 1) // 2:
            bwd = lax.ppermute(bwd, "z", behind)
        full = share(full, fwd, (z - step) % nz)
        if step <= (nz - 1) // 2:
            full = share(full, bwd, (z + step) % nz)
    return full


def ring_gather(block, axis, place, buf):
    n = lax.axis_size(axis)
    me = lax.axis_index(axis)
    ahead = [(i, (i + 1) % n) for i in range(n)]
    behind = [(i, (i - 1) % n) for i in range(n)]
    buf = place(buf, block, me)
    fwd = block
    bwd = block
    for step in range(1, n // 2 + 1):
        fwd = lax.ppermute(fwd, axis, ahead)
        if step <= (n - 1) // 2:
            bwd = lax.ppermute(bwd, axis, behind)
        buf = place(buf, fwd, (me - step) % n)
        if step <= (n - 1) // 2:
            buf = place(buf, bwd, (me + step) % n)
    return buf


def spread_gather(block, axis):
    n = lax.axis_size(axis)
    return lax.all_to_all(jnp.broadcast_to(block[None], (n,) + block.shape), axis, 0, 0, tiled=True)


def gather_head(head):
    depth, cols = head.shape
    nx = lax.axis_size("x")
    ny = lax.axis_size("y")
    half = (cols // 2) // 128 * 128
    strip = spread_gather(head[:, :half], "x").reshape(nx * depth, half)
    first_full = lax.all_gather(strip, "y", axis=0, tiled=True)

    width = cols - half

    def put_col(buf, piece, index):
        return lax.dynamic_update_slice(buf, piece[:, None], (0, index, 0, 0))

    column = spread_gather(head[:, half:], "y")
    second_full = ring_gather(column, "x", put_col, jnp.zeros((ny, nx, depth, width), head.dtype))
    return first_full, second_full.reshape(ny * nx * depth, width)


def local(hidden, head, targets, live, prior_lse, prior_mean, prior_target, seq_lengths):
    rows_here = hidden.shape[0]
    cols_here = head.shape[1]
    spread = lax.axis_size(VOCAB_AXES)
    which = lax.axis_index(VOCAB_AXES)
    block_first = VOCAB - cols_here * spread
    first_col = block_first + which * cols_here
    gathered = gather_hidden(hidden)
    head_first, head_second = gather_head(head)
    logits = jnp.concatenate(
        [
            jnp.dot(gathered, head_first, preferred_element_type=jnp.float32),
            jnp.dot(gathered, head_second, preferred_element_type=jnp.float32),
        ],
        axis=1,
    )
    row_peak = jnp.max(logits, axis=1)
    weights = jnp.exp(logits - row_peak[:, None])
    row_mass = jnp.sum(weights, axis=1)
    moment = jnp.sum(weights * logits, axis=1)
    column = targets - first_col
    columns = lax.broadcasted_iota(jnp.int32, logits.shape, 1)
    picked = jnp.sum(jnp.where(columns == column[:, None], logits, jnp.zeros_like(logits)), axis=1)

    stats = jnp.stack([row_peak, row_mass, moment, picked])
    copies = jnp.broadcast_to(stats[None], (spread,) + stats.shape)
    every = lax.all_to_all(copies, VOCAB_AXES, 0, 0, tiled=True)
    peaks = every[:, 0]
    highest = jnp.max(peaks, axis=0)
    factor = jnp.exp(peaks - highest[None, :])
    mass_all = jnp.sum(every[:, 1] * factor, axis=0)
    moment_all = jnp.sum(every[:, 2] * factor, axis=0)
    picked_all = jnp.sum(every[:, 3], axis=0)
    block_target = jnp.where(targets >= block_first, picked_all, prior_target)
    logprob, entropy = finish_rows(
        highest, mass_all, moment_all, block_target, live, prior_lse, prior_mean
    )

    share = rows_here // spread
    begin = which * share
    logprob_share = lax.dynamic_slice_in_dim(logprob, begin, share, 0)
    entropy_share = lax.dynamic_slice_in_dim(entropy, begin, share, 0)

    global_rows = lax.axis_index(ROW_AXES) * rows_here + jnp.arange(rows_here, dtype=jnp.int32)
    endings = jnp.cumsum(seq_lengths)
    member = jnp.sum((global_rows[:, None] >= endings[None, :]).astype(jnp.int32), axis=1)
    onehot = (member[:, None] == jnp.arange(SEQS, dtype=jnp.int32)[None, :]).astype(jnp.float32)
    partial_sums = jnp.sum(onehot * logprob[:, None], axis=0)
    peers = lax.axis_size(ROW_AXES)
    spread_sums = jnp.broadcast_to(partial_sums[None], (peers, SEQS))
    sums = jnp.sum(lax.all_to_all(spread_sums, ROW_AXES, 0, 0, tiled=True), axis=0)
    seq_mean = sums / seq_lengths.astype(jnp.float32)
    grouped = seq_mean.reshape(SEQS // GSIZE, GSIZE)
    seq_score = (grouped - jnp.mean(grouped, axis=1, keepdims=True)).reshape(SEQS)
    return (logprob_share, entropy_share, seq_score)


def solution(mesh):
    rows_y = 8 if mesh.shape["rows"] % 8 == 0 else 1
    vocab_c = 2 if mesh.shape["vocab"] % 2 == 0 else 1
    devices = mesh.devices.reshape(
        rows_y, mesh.shape["rows"] // rows_y, mesh.shape["vocab"] // vocab_c, vocab_c
    )
    fine = jax.sharding.Mesh(devices, ("y", "x", "z", "c"))
    rows, vocab = ROW_AXES, VOCAB_AXES
    return jax.shard_map(
        local,
        mesh=fine,
        in_specs=(
            P(rows, vocab),
            P(rows, vocab),
            P(rows),
            P(rows),
            P(rows),
            P(rows),
            P(rows),
            P(),
        ),
        out_specs=(P(rows + vocab), P(rows + vocab), P()),
        check_vma=False,
    )
```

```python
import jax
import jax.numpy as jnp
from jax import lax
from jax.sharding import PartitionSpec as P

VOCAB = 128256
SEQS = 32
GSIZE = 8
ROW_AXES = ("y", "x")
VOCAB_AXES = ("z", "c")


def finish_rows(block_peak, block_mass, block_moment, block_target, live, prior_lse, prior_mean):
    highest = jnp.maximum(block_peak, prior_lse)
    earlier = jnp.exp(prior_lse - highest)
    scaled = jnp.exp(block_peak - highest)
    total_mass = earlier + block_mass * scaled
    norm_log = highest + jnp.log(total_mass)
    average = (earlier * prior_mean + scaled * block_moment) / total_mass
    keeping = live.astype(jnp.float32)
    return (keeping * (block_target - norm_log), keeping * (norm_log - average))


def gather_hidden(hidden):
    rows, width = hidden.shape
    nz = lax.axis_size("z")
    nc = lax.axis_size("c")
    c = lax.axis_index("c")

    def put(buf, piece, index):
        return lax.dynamic_update_slice(buf, piece, (0, index * width))

    own = ring_gather(hidden, "z", put, jnp.zeros((rows, nz * width), hidden.dtype))
    if nc == 1:
        return own
    other = lax.ppermute(own, "c", [(i, (i + 1) % nc) for i in range(nc)])
    own = own.reshape(rows, nz, 1, width)
    other = other.reshape(rows, nz, 1, width)
    first = jnp.where(c == 0, own, other)
    second = jnp.where(c == 0, other, own)
    return jnp.concatenate([first, second], axis=2).reshape(rows, nz * nc * width)


def ring_gather(block, axis, place, buf):
    n = lax.axis_size(axis)
    me = lax.axis_index(axis)
    ahead = [(i, (i + 1) % n) for i in range(n)]
    behind = [(i, (i - 1) % n) for i in range(n)]
    buf = place(buf, block, me)
    fwd = block
    bwd = block
    for step in range(1, n // 2 + 1):
        fwd = lax.ppermute(fwd, axis, ahead)
        if step <= (n - 1) // 2:
            bwd = lax.ppermute(bwd, axis, behind)
        buf = place(buf, fwd, (me - step) % n)
        if step <= (n - 1) // 2:
            buf = place(buf, bwd, (me + step) % n)
    return buf


def spread_gather(block, axis):
    n = lax.axis_size(axis)
    return lax.all_to_all(jnp.broadcast_to(block[None], (n,) + block.shape), axis, 0, 0, tiled=True)


def gather_head(head):
    depth, cols = head.shape
    nx = lax.axis_size("x")
    ny = lax.axis_size("y")
    half = (cols * 3 // 4) // 128 * 128
    strip = spread_gather(head[:, :half], "x").reshape(nx * depth, half)
    first_full = lax.all_gather(strip, "y", axis=0, tiled=True)

    width = cols - half

    def put_col(buf, piece, index):
        return lax.dynamic_update_slice(buf, piece[:, None], (0, index, 0, 0))

    column = spread_gather(head[:, half:], "y")
    second_full = ring_gather(column, "x", put_col, jnp.zeros((ny, nx, depth, width), head.dtype))
    return first_full, second_full.reshape(ny * nx * depth, width)


def local(hidden, head, targets, live, prior_lse, prior_mean, prior_target, seq_lengths):
    rows_here = hidden.shape[0]
    cols_here = head.shape[1]
    spread = lax.axis_size(VOCAB_AXES)
    which = lax.axis_index(VOCAB_AXES)
    block_first = VOCAB - cols_here * spread
    first_col = block_first + which * cols_here
    gathered = gather_hidden(hidden)
    head_first, head_second = gather_head(head)
    logits = jnp.concatenate(
        [
            jnp.dot(gathered, head_first, preferred_element_type=jnp.float32),
            jnp.dot(gathered, head_second, preferred_element_type=jnp.float32),
        ],
        axis=1,
    )
    row_peak = jnp.max(logits, axis=1)
    weights = jnp.exp(logits - row_peak[:, None])
    row_mass = jnp.sum(weights, axis=1)
    moment = jnp.sum(weights * logits, axis=1)
    column = targets - first_col
    columns = lax.broadcasted_iota(jnp.int32, logits.shape, 1)
    picked = jnp.sum(jnp.where(columns == column[:, None], logits, jnp.zeros_like(logits)), axis=1)

    stats = jnp.stack([row_peak, row_mass, moment, picked])
    copies = jnp.broadcast_to(stats[None], (spread,) + stats.shape)
    every = lax.all_to_all(copies, VOCAB_AXES, 0, 0, tiled=True)
    peaks = every[:, 0]
    highest = jnp.max(peaks, axis=0)
    factor = jnp.exp(peaks - highest[None, :])
    mass_all = jnp.sum(every[:, 1] * factor, axis=0)
    moment_all = jnp.sum(every[:, 2] * factor, axis=0)
    picked_all = jnp.sum(every[:, 3], axis=0)
    block_target = jnp.where(targets >= block_first, picked_all, prior_target)
    logprob, entropy = finish_rows(
        highest, mass_all, moment_all, block_target, live, prior_lse, prior_mean
    )

    share = rows_here // spread
    begin = which * share
    logprob_share = lax.dynamic_slice_in_dim(logprob, begin, share, 0)
    entropy_share = lax.dynamic_slice_in_dim(entropy, begin, share, 0)

    global_rows = lax.axis_index(ROW_AXES) * rows_here + jnp.arange(rows_here, dtype=jnp.int32)
    endings = jnp.cumsum(seq_lengths)
    member = jnp.sum((global_rows[:, None] >= endings[None, :]).astype(jnp.int32), axis=1)
    onehot = (member[:, None] == jnp.arange(SEQS, dtype=jnp.int32)[None, :]).astype(jnp.float32)
    partial_sums = jnp.sum(onehot * logprob[:, None], axis=0)
    peers = lax.axis_size(ROW_AXES)
    spread_sums = jnp.broadcast_to(partial_sums[None], (peers, SEQS))
    sums = jnp.sum(lax.all_to_all(spread_sums, ROW_AXES, 0, 0, tiled=True), axis=0)
    seq_mean = sums / seq_lengths.astype(jnp.float32)
    grouped = seq_mean.reshape(SEQS // GSIZE, GSIZE)
    seq_score = (grouped - jnp.mean(grouped, axis=1, keepdims=True)).reshape(SEQS)
    return (logprob_share, entropy_share, seq_score)


def solution(mesh):
    rows_y = 8 if mesh.shape["rows"] % 8 == 0 else 1
    vocab_c = 2 if mesh.shape["vocab"] % 2 == 0 else 1
    devices = mesh.devices.reshape(
        rows_y, mesh.shape["rows"] // rows_y, mesh.shape["vocab"] // vocab_c, vocab_c
    )
    fine = jax.sharding.Mesh(devices, ("y", "x", "z", "c"))
    rows, vocab = ROW_AXES, VOCAB_AXES
    return jax.shard_map(
        local,
        mesh=fine,
        in_specs=(
            P(rows, vocab),
            P(rows, vocab),
            P(rows),
            P(rows),
            P(rows),
            P(rows),
            P(rows),
            P(),
        ),
        out_specs=(P(rows + vocab), P(rows + vocab), P()),
        check_vma=False,
    )
```

```python
import jax
import jax.numpy as jnp
from jax import lax
from jax.sharding import PartitionSpec as P

VOCAB = 128256
SEQS = 32
GSIZE = 8
ROW_AXES = ("y", "x_hi", "x_lo")
VOCAB_AXES = ("z", "c")


def finish_rows(block_peak, block_mass, block_moment, block_target, live, prior_lse, prior_mean):
    highest = jnp.maximum(block_peak, prior_lse)
    earlier = jnp.exp(prior_lse - highest)
    scaled = jnp.exp(block_peak - highest)
    total_mass = earlier + block_mass * scaled
    norm_log = highest + jnp.log(total_mass)
    average = (earlier * prior_mean + scaled * block_moment) / total_mass
    keeping = live.astype(jnp.float32)
    return (keeping * (block_target - norm_log), keeping * (norm_log - average))


def gather_hidden(hidden):
    nz = lax.axis_size("z")
    z = lax.axis_index("z")
    c = lax.axis_index("c")
    nc = lax.axis_size("c")
    width = hidden.shape[1]
    ahead = [(i, (i + 1) % nz) for i in range(nz)]
    behind = [(i, (i - 1) % nz) for i in range(nz)]
    across = [(i, (i + 1) % nc) for i in range(nc)]
    full = jnp.zeros((hidden.shape[0], width * nz * nc), hidden.dtype)

    def place(buf, piece, chip, core):
        slot = (chip * nc + core) * width
        return lax.dynamic_update_slice(buf, piece, (0, slot))

    def share(buf, piece, chip):
        buf = place(buf, piece, chip, c)
        if nc > 1:
            other = lax.ppermute(piece, "c", across)
            buf = place(buf, other, chip, (c + 1) % nc)
        return buf

    full = share(full, hidden, z)
    fwd = hidden
    bwd = hidden
    for step in range(1, nz // 2 + 1):
        fwd = lax.ppermute(fwd, "z", ahead)
        if step <= (nz - 1) // 2:
            bwd = lax.ppermute(bwd, "z", behind)
        full = share(full, fwd, (z - step) % nz)
        if step <= (nz - 1) // 2:
            full = share(full, bwd, (z + step) % nz)
    return full


def gather_head(head):
    n = lax.axis_size("x_lo")
    lo = lax.axis_index("x_lo")
    other = lax.ppermute(head, "x_lo", [(i, i ^ 1) for i in range(n)])
    pair = jnp.where(
        lo % 2 == 0,
        jnp.concatenate([head, other], axis=0),
        jnp.concatenate([other, head], axis=0),
    )
    return lax.all_gather(pair, ("y", "x_hi"), axis=0, tiled=True)


def local(hidden, head, targets, live, prior_lse, prior_mean, prior_target, seq_lengths):
    rows_here = hidden.shape[0]
    cols_here = head.shape[1]
    spread = lax.axis_size(VOCAB_AXES)
    which = lax.axis_index(VOCAB_AXES)
    block_first = VOCAB - cols_here * spread
    first_col = block_first + which * cols_here
    gathered = gather_hidden(hidden)
    logits = jnp.dot(
        gathered,
        gather_head(head),
        preferred_element_type=jnp.float32,
    )
    row_peak = jnp.max(logits, axis=1)
    weights = jnp.exp(logits - row_peak[:, None])
    row_mass = jnp.sum(weights, axis=1)
    moment = jnp.sum(weights * logits, axis=1)
    column = targets - first_col
    columns = lax.broadcasted_iota(jnp.int32, logits.shape, 1)
    picked = jnp.sum(jnp.where(columns == column[:, None], logits, jnp.zeros_like(logits)), axis=1)

    stats = jnp.stack([row_peak, row_mass, moment, picked])
    copies = jnp.broadcast_to(stats[None], (spread,) + stats.shape)
    every = lax.all_to_all(copies, VOCAB_AXES, 0, 0, tiled=True)
    peaks = every[:, 0]
    highest = jnp.max(peaks, axis=0)
    factor = jnp.exp(peaks - highest[None, :])
    mass_all = jnp.sum(every[:, 1] * factor, axis=0)
    moment_all = jnp.sum(every[:, 2] * factor, axis=0)
    picked_all = jnp.sum(every[:, 3], axis=0)
    block_target = jnp.where(targets >= block_first, picked_all, prior_target)
    logprob, entropy = finish_rows(
        highest, mass_all, moment_all, block_target, live, prior_lse, prior_mean
    )

    share = rows_here // spread
    begin = which * share
    logprob_share = lax.dynamic_slice_in_dim(logprob, begin, share, 0)
    entropy_share = lax.dynamic_slice_in_dim(entropy, begin, share, 0)

    global_rows = lax.axis_index(ROW_AXES) * rows_here + jnp.arange(rows_here, dtype=jnp.int32)
    endings = jnp.cumsum(seq_lengths)
    member = jnp.sum((global_rows[:, None] >= endings[None, :]).astype(jnp.int32), axis=1)
    onehot = (member[:, None] == jnp.arange(SEQS, dtype=jnp.int32)[None, :]).astype(jnp.float32)
    partial_sums = jnp.sum(onehot * logprob[:, None], axis=0)
    peers = lax.axis_size(ROW_AXES)
    spread_sums = jnp.broadcast_to(partial_sums[None], (peers, SEQS))
    sums = jnp.sum(lax.all_to_all(spread_sums, ROW_AXES, 0, 0, tiled=True), axis=0)
    seq_mean = sums / seq_lengths.astype(jnp.float32)
    grouped = seq_mean.reshape(SEQS // GSIZE, GSIZE)
    seq_score = (grouped - jnp.mean(grouped, axis=1, keepdims=True)).reshape(SEQS)
    return (logprob_share, entropy_share, seq_score)


def solution(mesh):
    rows_y = 8 if mesh.shape["rows"] % 8 == 0 else 1
    vocab_c = 2 if mesh.shape["vocab"] % 2 == 0 else 1
    devices = mesh.devices.reshape(
        rows_y, mesh.shape["rows"] // rows_y // 2, 2, mesh.shape["vocab"] // vocab_c, vocab_c
    )
    fine = jax.sharding.Mesh(devices, ("y", "x_hi", "x_lo", "z", "c"))
    rows, vocab = ROW_AXES, VOCAB_AXES
    return jax.shard_map(
        local,
        mesh=fine,
        in_specs=(
            P(rows, vocab),
            P(rows, vocab),
            P(rows),
            P(rows),
            P(rows),
            P(rows),
            P(rows),
            P(),
        ),
        out_specs=(P(rows + vocab), P(rows + vocab), P()),
        check_vma=False,
    )
```
